512 devices in a mesh: dp: 32 (over x, z), mp: 16 (over y, core).
Axes of the slice: x: 4, y: 8, z: 8, core: 2. Of those that a mesh axis runs over, the one named last changes fastest.
Arguments:
- hidden_rows: bfloat16 [16384, 8192], P('dp', 'mp'), may hold values from -6 to 6
- base_weight: bfloat16 [8192, 4096], P('mp'), may hold values from -0.0625 to 0.0625
- adapter_down: bfloat16 [32, 64, 8192], P('dp', None, 'mp'), may hold values from -0.0625 to 0.0625
- adapter_up: bfloat16 [32, 64, 4096], P('dp', None, 'mp'), may hold values from -0.75 to 0.75
- adapter_of_row: int32 [16384, 1], P('dp'), may hold values from 0 to 31; in each aligned block of 512 rows (0 to 511, 512 to 1023, ...) at most 32 rows name the same one
- holder_map: int32 [32], replicated, may hold values from 0 to 31, each once
Outputs:
- projected: bfloat16 [16384, 4096], P('dp', 'mp')
The draws below stay inside these ranges and needn't reach their ends.
Inputs may be any that keep to these rules, and one draw needn't show every extreme that they name: `adapter_of_row`: within the 512 rows of one index of dp (aligned blocks), no adapter is named by more than 32 rows; every adapter is named by some row. `holder_map`: each of the 32 slots holds exactly one adapter.
All inputs are finite; a program needn't handle non-finite values.
Results may differ from the reference program's by a relative error of at most 0.02.
Values may be sent and summed in bfloat16 or wider, within the bound.
No kernel may reach another device: no remote copies, remote signals or barrier semaphores. Data moves between devices by JAX's collectives and lax.ppermute only.
A program may use at most 64 MiB of HBM per device.

```python
import math
import jax
import jax.numpy as jnp
import numpy as np
from jax import lax

D = 8192
DOUT = 4096
RANK = 64
ROWS_DEV = 512
ROWS = 16384
ADAPTERS = 32
CAP = 32
N_MP = 16


def level_of(stream_key, shape, cuts, low, largest):
    def one(dim, parts):
        draws = jax.random.uniform(jax.random.fold_in(jax.random.fold_in(stream_key, 6), dim), (parts,), jnp.float32, low / len(cuts), largest / len(cuts))
        return jnp.repeat(jnp.exp(draws), shape[dim] // parts).reshape((-1,) + (1,) * (len(shape) - dim - 1))

    gain = one(*cuts[0])
    for cut in cuts[1:]:
        gain = gain * one(*cut)
    return gain


def assign_block(stream_key, own, number, rows, amount, top, limit, slope):
    order = jax.random.permutation(stream_key, amount)
    crowded, usual = portions_of(amount, rows * top, limit, slope, True), portions_of(amount, rows * top, limit, slope, False)
    places = jnp.arange(amount)

    def named(lengths, turn):
        used = int((lengths > 0).sum())
        fixed = max(1, used // 4)
        shifted = fixed + (places - fixed + turn * (used - fixed)) % max(1, amount - fixed)
        return jnp.zeros((amount,), jnp.int32).at[order[jnp.where(places < fixed, places, shifted)]].set(jnp.asarray(lengths, jnp.int32))

    lengths = jnp.where(number % 4 == 0, named(crowded, number // 4), named(usual, number - number // 4 - 1))
    mixed = jax.random.permutation(jax.random.fold_in(own, 3), amount)
    donor, sink = mixed[0:amount // 2 * 2:2], mixed[1:amount // 2 * 2:2]
    margin = jnp.minimum(lengths[donor] - 1, limit - lengths[sink]) // 2
    margin = jnp.where((donor == order[0]) | (sink == order[0]) | (lengths[sink] == 0), 0, jnp.maximum(margin, 0))
    shifted = jax.random.randint(jax.random.fold_in(own, 4), (amount // 2,), 0, 1 << 20) % (margin + 1)
    lengths = lengths.at[donor].add(-shifted).at[sink].add(shifted)
    members = jnp.searchsorted(jnp.cumsum(lengths), jnp.arange(rows * top), side="right").astype(jnp.int32)
    listing = members.reshape(top, rows).T
    listing = listing[jax.random.permutation(jax.random.fold_in(own, 1), rows)]
    turn = jax.random.randint(jax.random.fold_in(own, 2), (rows, 1), 0, top)
    return jnp.take_along_axis(listing, (jnp.arange(top)[None, :] + turn) % top, axis=1)


def portions_of(amount, total, bound, slope, full):
    portions = [(1 << 20) // math.isqrt(grade ** slope) + 1 for grade in range(1, amount + 1)]
    largest = bound if full else min(bound, max(-(-total // amount), total * portions[0] // sum(portions)))
    least = 1 if total - largest >= amount - 1 else 0
    holding, rest = [largest] + [least] * (amount - 1), total - largest - least * (amount - 1)
    while rest > 0:
        candidates = [i for i in range(1, amount) if holding[i] < largest] or [i for i in range(1, amount) if holding[i] < bound]
        mass, remaining = sum([portions[i] for i in candidates]), rest
        for i in candidates:
            addition = min(bound - holding[i], max(1, remaining * portions[i] // mass), rest)
            holding[i] = holding[i] + addition
            rest = rest - addition
    return np.array(holding)


def gaussian(rng, extent, scale, most, pieces=(), kind=jnp.bfloat16):
    array = jax.random.normal(rng, extent, jnp.float32) * scale
    if len(pieces) > 0:
        array = level_of(rng, extent, pieces, -0.22, 0.18) * array
    return jnp.clip(array, min=-most, max=most).astype(kind)


def setup_inputs(seed: int = 0) -> dict:
    streams_of = jax.random.split(jax.random.key(seed), 7)
    hidden_rows = gaussian(streams_of[0], (ROWS, D), 1.0, 6.0, ((0, 32), (1, 16)))
    base_weight = gaussian(streams_of[1], (D, DOUT), D ** -0.5, 0.0625, ((0, 16),))
    adapter_down = gaussian(streams_of[2], (ADAPTERS, RANK, D), D ** -0.5, 0.0625, ((0, 32), (2, 16)))
    adapter_up = gaussian(streams_of[3], (ADAPTERS, RANK, DOUT), RANK ** -0.5, 0.75, ((0, 32), (2, 16)))
    adapter_of_row_keys = jax.random.split(jax.random.fold_in(streams_of[4], 1), ROWS // ROWS_DEV)
    adapter_of_row_turns = jax.random.permutation(jax.random.fold_in(streams_of[4], 3), ROWS // ROWS_DEV)
    adapter_of_row = jax.vmap(lambda own, number: assign_block(jax.random.fold_in(streams_of[4], 2), own, number, ROWS_DEV, ADAPTERS, 1, CAP, 2))(adapter_of_row_keys, adapter_of_row_turns).reshape((ROWS, 1))
    holder_map = jax.random.permutation(streams_of[5], ADAPTERS).astype(jnp.int32)
    return {"hidden_rows": hidden_rows, "base_weight": base_weight, "adapter_down": adapter_down, "adapter_up": adapter_up, "adapter_of_row": adapter_of_row, "holder_map": holder_map}


def reference(hidden_rows, base_weight, adapter_down, adapter_up, adapter_of_row, holder_map):
    row_total = hidden_rows.shape[0]
    feat_width = D // N_MP
    slot_of_row = holder_map[adapter_of_row[:, 0]].astype(jnp.int32)
    row_blocks = hidden_rows.reshape(row_total, N_MP, feat_width).transpose(1, 0, 2)
    weight_blocks = base_weight.reshape(N_MP, feat_width, DOUT)

    def add_block(total, pair):
        partial_value = jnp.dot(pair[0], pair[1], preferred_element_type=jnp.float32)
        rounded = lax.optimization_barrier(partial_value.astype(jnp.bfloat16))
        return total + rounded.astype(jnp.float32), None

    base, _ = lax.scan(add_block, jnp.zeros((row_total, DOUT), jnp.float32), (row_blocks, weight_blocks))

    def adapter_block(pair):
        block_rows, block_slots = pair
        down_mats = adapter_down[block_slots].astype(jnp.float32)
        reduced = jnp.einsum("rd,rkd->rk", block_rows.astype(jnp.float32), down_mats).astype(jnp.bfloat16)
        up_mats = adapter_up[block_slots].astype(jnp.float32)
        return jnp.einsum("rk,rko->ro", reduced.astype(jnp.float32), up_mats).astype(jnp.bfloat16)

    lifted = lax.map(adapter_block, (hidden_rows.reshape(-1, 32, D), slot_of_row.reshape(-1, 32)))
    lifted = lifted.reshape(row_total, DOUT)
    return (base + lifted.astype(jnp.float32)).astype(jnp.bfloat16)
```

```python
import jax
import jax.numpy as jnp
from jax import lax
from jax.sharding import PartitionSpec as P


def per_device(hidden_rows, base_weight, adapter_down, adapter_up, adapter_of_row, holder_map):
    row_count, feat_width = hidden_rows.shape
    holders = lax.axis_size("dp")
    n_mp = lax.axis_size("mp")
    rank = adapter_down.shape[1]
    out_width = adapter_up.shape[2]
    adapters = holder_map.shape[0]

    adapter_ids = adapter_of_row[:, 0]
    matches = adapter_ids[:, None] == jnp.arange(adapters, dtype=jnp.int32)[None, :]
    slot_of_row = jnp.sum(jnp.where(matches, holder_map[None, :], 0), axis=1)
    slot_hot = slot_of_row[:, None] == jnp.arange(holders, dtype=jnp.int32)[None, :]

    both = jnp.concatenate([adapter_down[0], adapter_up[0]], axis=1)
    stack = lax.all_gather(both, "dp", axis=0, tiled=False)
    down_w = stack[:, :, :feat_width]
    up_w = stack[:, :, feat_width:]

    base_terms = jnp.dot(hidden_rows, base_weight, preferred_element_type=jnp.float32)
    base_bf = base_terms.astype(jnp.bfloat16)
    base_bf, stack = lax.optimization_barrier((base_bf, stack))
    base_total = lax.psum_scatter(base_bf, "mp", scatter_dimension=1, tiled=True).astype(
        jnp.float32
    )

    every = jnp.dot(
        hidden_rows,
        down_w.transpose(2, 0, 1).reshape(feat_width, holders * rank),
        preferred_element_type=jnp.float32,
    ).reshape(row_count, holders, rank)
    partial_down = jnp.sum(jnp.where(slot_hot[:, :, None], every, 0.0), axis=1)
    spread = jnp.broadcast_to(partial_down.astype(jnp.bfloat16)[None], (n_mp, row_count, rank))
    gathered = lax.all_to_all(spread, "mp", 0, 0, tiled=False)
    down = jnp.sum(gathered.astype(jnp.float32), axis=0).astype(jnp.bfloat16)

    placed = jnp.where(slot_hot[:, :, None], down[:, None, :], jnp.zeros((), jnp.bfloat16))
    lift = jnp.dot(
        placed.reshape(row_count, holders * rank),
        up_w.reshape(holders * rank, out_width),
        preferred_element_type=jnp.float32,
    ).astype(jnp.bfloat16)
    return (base_total + lift.astype(jnp.float32)).astype(jnp.bfloat16)


def solution(mesh):
    placed = (
        P("dp", "mp"),
        P("mp", None),
        P("dp", None, "mp"),
        P("dp", None, "mp"),
        P("dp", None),
        P(),
    )
    return jax.shard_map(
        per_device, mesh=mesh, in_specs=placed, out_specs=P("dp", "mp"), check_vma=False
    )
```

```python
import jax
import jax.numpy as jnp
from jax import lax
from jax.sharding import PartitionSpec as P


def per_device(hidden_rows, base_weight, adapter_down, adapter_up, adapter_of_row, holder_map):
    row_count, feat_width = hidden_rows.shape
    holders = lax.axis_size("dp")
    n_mp = lax.axis_size("mp")
    rank = adapter_down.shape[1]
    out_width = adapter_up.shape[2]
    adapters = holder_map.shape[0]

    adapter_ids = adapter_of_row[:, 0]
    matches = adapter_ids[:, None] == jnp.arange(adapters, dtype=jnp.int32)[None, :]
    slot_of_row = jnp.sum(jnp.where(matches, holder_map[None, :], 0), axis=1)
    slot_hot = slot_of_row[:, None] == jnp.arange(holders, dtype=jnp.int32)[None, :]

    base_terms = jnp.dot(hidden_rows, base_weight, preferred_element_type=jnp.float32)
    base_bf = base_terms.astype(jnp.bfloat16)
    base_total = lax.psum_scatter(base_bf, "mp", scatter_dimension=1, tiled=True).astype(
        jnp.float32
    )

    both = jnp.concatenate([adapter_down[0], adapter_up[0]], axis=1)
    base_bf, both = lax.optimization_barrier((base_bf, both))
    spread_w = jnp.broadcast_to(both[None], (holders,) + both.shape)
    stack = lax.all_to_all(spread_w, "dp", 0, 0, tiled=False)
    down_w = stack[:, :, :feat_width]
    up_w = stack[:, :, feat_width:]

    every = jnp.dot(
        hidden_rows,
        down_w.transpose(2, 0, 1).reshape(feat_width, holders * rank),
        preferred_element_type=jnp.float32,
    ).reshape(row_count, holders, rank)
    partial_down = jnp.sum(jnp.where(slot_hot[:, :, None], every, 0.0), axis=1)
    spread = jnp.broadcast_to(partial_down.astype(jnp.bfloat16)[None], (n_mp, row_count, rank))
    gathered = lax.all_to_all(spread, "mp", 0, 0, tiled=False)
    down = jnp.sum(gathered.astype(jnp.float32), axis=0).astype(jnp.bfloat16)

    placed = jnp.where(slot_hot[:, :, None], down[:, None, :], jnp.zeros((), jnp.bfloat16))
    lift = jnp.dot(
        placed.reshape(row_count, holders * rank),
        up_w.reshape(holders * rank, out_width),
        preferred_element_type=jnp.float32,
    ).astype(jnp.bfloat16)
    return (base_total + lift.astype(jnp.float32)).astype(jnp.bfloat16)


def solution(mesh):
    placed = (
        P("dp", "mp"),
        P("mp", None),
        P("dp", None, "mp"),
        P("dp", None, "mp"),
        P("dp", None),
        P(),
    )
    return jax.shard_map(
        per_device, mesh=mesh, in_specs=placed, out_specs=P("dp", "mp"), check_vma=False
    )
```

```python
import jax
import jax.numpy as jnp
import numpy as np
from jax import lax
from jax.sharding import Mesh, PartitionSpec as P


def spread_over(block, axis):
    n = lax.axis_size(axis)
    return lax.all_to_all(jnp.broadcast_to(block[None], (n,) + block.shape), axis, 0, 0, tiled=False)


def split_axis(mesh, name):
    lead = [slice(None) if a == name else 0 for a in mesh.axis_names]
    line = mesh.devices[tuple(lead)].reshape(-1)
    parts = []
    for c in range(3):
        n = len({d.coords[c] for d in line})
        if n > 1:
            parts.append((c, n))
    if len({d.core_on_chip for d in line}) > 1:
        parts.append((3, 2))
    return parts


def per_device(hidden_rows, base_weight, adapter_down, adapter_up, adapter_of_row, holder_map):
    row_count, feat_width = hidden_rows.shape
    holders = lax.axis_size(DP)
    n_mp = lax.axis_size(MP)
    rank = adapter_down.shape[1]
    out_width = adapter_up.shape[2]
    adapters = holder_map.shape[0]

    adapter_ids = adapter_of_row[:, 0]
    matches = adapter_ids[:, None] == jnp.arange(adapters, dtype=jnp.int32)[None, :]
    slot_of_row = jnp.sum(jnp.where(matches, holder_map[None, :], 0), axis=1)
    slot_hot = slot_of_row[:, None] == jnp.arange(holders, dtype=jnp.int32)[None, :]

    base_terms = jnp.dot(hidden_rows, base_weight, preferred_element_type=jnp.float32)
    base_bf = base_terms.astype(jnp.bfloat16)
    base_total = lax.psum_scatter(base_bf, MP, scatter_dimension=1, tiled=True).astype(
        jnp.float32
    )

    both = jnp.concatenate([adapter_down[0], adapter_up[0]], axis=1)[None]
    for axis in reversed(DP):
        both = spread_over(both, axis)
    stack = both.reshape(holders, rank, both.shape[-1])
    down_w = stack[:, :, :feat_width]
    up_w = stack[:, :, feat_width:]

    every = jnp.dot(
        hidden_rows,
        down_w.transpose(2, 0, 1).reshape(feat_width, holders * rank),
        preferred_element_type=jnp.float32,
    ).reshape(row_count, holders, rank)
    partial_down = jnp.sum(jnp.where(slot_hot[:, :, None], every, 0.0), axis=1)
    gathered = partial_down.astype(jnp.bfloat16)[None]
    for axis in MP:
        gathered = spread_over(gathered, axis)
    gathered = gathered.reshape(n_mp, row_count, rank)
    down = jnp.sum(gathered.astype(jnp.float32), axis=0).astype(jnp.bfloat16)

    placed = jnp.where(slot_hot[:, :, None], down[:, None, :], jnp.zeros((), jnp.bfloat16))
    lift = jnp.dot(
        placed.reshape(row_count, holders * rank),
        up_w.reshape(holders * rank, out_width),
        preferred_element_type=jnp.float32,
    ).astype(jnp.bfloat16)
    return (base_total + lift.astype(jnp.float32)).astype(jnp.bfloat16)


def coordinate(device, c):
    return device.core_on_chip if c == 3 else device.coords[c]


def fine_mesh(mesh):
    parts = [split_axis(mesh, name) for name in mesh.axis_names]
    names = [tuple(f"{name}{c}" for c, _ in p) for name, p in zip(mesh.axis_names, parts)]
    flat = [q for p in parts for q in p]
    devices = mesh.devices.reshape([n for _, n in flat])
    for k, (c, n) in enumerate(flat):
        for index in np.ndindex(devices.shape):
            if index[k] + 1 < n:
                step = list(index)
                step[k] += 1
                a, b = devices[index], devices[tuple(step)]
                if any((coordinate(a, o) != coordinate(b, o)) != (o == c) for o in range(4)):
                    return mesh, tuple((name,) for name in mesh.axis_names)
    return Mesh(devices, tuple(q for p in names for q in p)), tuple(names)


def solution(mesh):
    global DP, MP
    fine, (DP, MP) = fine_mesh(mesh)
    placed = (
        P(DP, MP),
        P(MP, None),
        P(DP, None, MP),
        P(DP, None, MP),
        P(DP, None),
        P(),
    )
    return jax.shard_map(per_device, mesh=fine, in_specs=placed, out_specs=P(DP, MP), check_vma=False)
```

```python
import jax
import jax.numpy as jnp
import numpy as np
from jax import lax
from jax.sharding import Mesh, PartitionSpec as P


def spread_over(block, axis):
    n = lax.axis_size(axis)
    return lax.all_to_all(jnp.broadcast_to(block[None], (n,) + block.shape), axis, 0, 0, tiled=False)


def split_axis(mesh, name):
    lead = [slice(None) if a == name else 0 for a in mesh.axis_names]
    line = mesh.devices[tuple(lead)].reshape(-1)
    parts = []
    for c in range(3):
        n = len({d.coords[c] for d in line})
        if n > 1:
            parts.append((c, n))
    if len({d.core_on_chip for d in line}) > 1:
        parts.append((3, 2))
    return parts


def per_device(hidden_rows, base_weight, adapter_down, adapter_up, adapter_of_row, holder_map):
    row_count, feat_width = hidden_rows.shape
    holders = lax.axis_size(DP)
    n_mp = lax.axis_size(MP)
    rank = adapter_down.shape[1]
    out_width = adapter_up.shape[2]
    adapters = holder_map.shape[0]

    adapter_ids = adapter_of_row[:, 0]
    matches = adapter_ids[:, None] == jnp.arange(adapters, dtype=jnp.int32)[None, :]
    slot_of_row = jnp.sum(jnp.where(matches, holder_map[None, :], 0), axis=1)
    slot_hot = slot_of_row[:, None] == jnp.arange(holders, dtype=jnp.int32)[None, :]

    both = jnp.concatenate([adapter_down[0], adapter_up[0]], axis=1)[None]
    for axis in reversed(DP):
        if axis == DP[-1] and len(DP) > 1:
            both = lax.all_gather(both, axis, axis=0, tiled=False)
            first_stage = both
        else:
            both = spread_over(both, axis)
    stack = both.reshape(holders, rank, both.shape[-1])
    down_w = stack[:, :, :feat_width]
    up_w = stack[:, :, feat_width:]

    base_terms = jnp.dot(hidden_rows, base_weight, preferred_element_type=jnp.float32)
    base_bf = base_terms.astype(jnp.bfloat16)
    if len(DP) > 1:
        base_bf, first_stage = lax.optimization_barrier((base_bf, first_stage))
    base_total = lax.psum_scatter(base_bf, MP, scatter_dimension=1, tiled=True).astype(
        jnp.float32
    )

    every = jnp.dot(
        hidden_rows,
        down_w.transpose(2, 0, 1).reshape(feat_width, holders * rank),
        preferred_element_type=jnp.float32,
    ).reshape(row_count, holders, rank)
    partial_down = jnp.sum(jnp.where(slot_hot[:, :, None], every, 0.0), axis=1)
    gathered = partial_down.astype(jnp.bfloat16)[None]
    for axis in MP:
        gathered = spread_over(gathered, axis)
    gathered = gathered.reshape(n_mp, row_count, rank)
    down = jnp.sum(gathered.astype(jnp.float32), axis=0).astype(jnp.bfloat16)

    placed = jnp.where(slot_hot[:, :, None], down[:, None, :], jnp.zeros((), jnp.bfloat16))
    lift = jnp.dot(
        placed.reshape(row_count, holders * rank),
        up_w.reshape(holders * rank, out_width),
        preferred_element_type=jnp.float32,
    ).astype(jnp.bfloat16)
    return (base_total + lift.astype(jnp.float32)).astype(jnp.bfloat16)


def coordinate(device, c):
    return device.core_on_chip if c == 3 else device.coords[c]


def fine_mesh(mesh):
    parts = [split_axis(mesh, name) for name in mesh.axis_names]
    names = [tuple(f"{name}{c}" for c, _ in p) for name, p in zip(mesh.axis_names, parts)]
    flat = [q for p in parts for q in p]
    devices = mesh.devices.reshape([n for _, n in flat])
    for k, (c, n) in enumerate(flat):
        for index in np.ndindex(devices.shape):
            if index[k] + 1 < n:
                step = list(index)
                step[k] += 1
                a, b = devices[index], devices[tuple(step)]
                if any((coordinate(a, o) != coordinate(b, o)) != (o == c) for o in range(4)):
                    return mesh, tuple((name,) for name in mesh.axis_names)
    return Mesh(devices, tuple(q for p in names for q in p)), tuple(names)


def solution(mesh):
    global DP, MP
    fine, (DP, MP) = fine_mesh(mesh)
    placed = (
        P(DP, MP),
        P(MP, None),
        P(DP, None, MP),
        P(DP, None, MP),
        P(DP, None),
        P(),
    )
    return jax.shard_map(per_device, mesh=fine, in_specs=placed, out_specs=P(DP, MP), check_vma=False)
```

```python
import jax
import jax.numpy as jnp
import numpy as np
from jax import lax
from jax.sharding import Mesh, PartitionSpec as P


def spread_over(block, axis):
    n = lax.axis_size(axis)
    return lax.all_to_all(jnp.broadcast_to(block[None], (n,) + block.shape), axis, 0, 0, tiled=False)


def split_axis(mesh, name):
    lead = [slice(None) if a == name else 0 for a in mesh.axis_names]
    line = mesh.devices[tuple(lead)].reshape(-1)
    parts = []
    for c in range(3):
        n = len({d.coords[c] for d in line})
        if n > 1:
            parts.append((c, n))
    if len({d.core_on_chip for d in line}) > 1:
        parts.append((3, 2))
    return parts


def per_device(hidden_rows, base_weight, adapter_down, adapter_up, adapter_of_row, holder_map):
    row_count, feat_width = hidden_rows.shape
    holders = lax.axis_size(DP)
    n_mp = lax.axis_size(MP)
    rank = adapter_down.shape[1]
    out_width = adapter_up.shape[2]
    adapters = holder_map.shape[0]

    adapter_ids = adapter_of_row[:, 0]
    matches = adapter_ids[:, None] == jnp.arange(adapters, dtype=jnp.int32)[None, :]
    slot_of_row = jnp.sum(jnp.where(matches, holder_map[None, :], 0), axis=1)
    slot_hot = slot_of_row[:, None] == jnp.arange(holders, dtype=jnp.int32)[None, :]

    both = jnp.concatenate([adapter_down[0], adapter_up[0]], axis=1)[None]
    for axis in reversed(DP):
        if axis == DP[-1] and len(DP) > 1:
            both = lax.all_gather(both, axis, axis=0, tiled=False)
            first_stage = both
        else:
            both = spread_over(both, axis)
    stack = both.reshape(holders, rank, both.shape[-1])
    down_w = stack[:, :, :feat_width]
    up_w = stack[:, :, feat_width:]

    base_terms = jnp.dot(hidden_rows, base_weight, preferred_element_type=jnp.float32)
    base_bf = base_terms.astype(jnp.bfloat16)
    if len(DP) > 1:
        base_bf, first_stage = lax.optimization_barrier((base_bf, first_stage))
    base_total = lax.psum_scatter(base_bf, MP, scatter_dimension=1, tiled=True).astype(
        jnp.float32
    )

    every = jnp.dot(
        hidden_rows,
        down_w.transpose(2, 0, 1).reshape(feat_width, holders * rank),
        preferred_element_type=jnp.float32,
    ).reshape(row_count, holders, rank)
    partial_down = jnp.sum(jnp.where(slot_hot[:, :, None], every, 0.0), axis=1)
    gathered = partial_down.astype(jnp.bfloat16)[None]
    for axis in MP:
        if axis == MP[0] and len(MP) > 1:
            gathered = lax.all_gather(gathered, axis, axis=0, tiled=False)
        else:
            gathered = spread_over(gathered, axis)
    gathered = gathered.reshape(n_mp, row_count, rank)
    down = jnp.sum(gathered.astype(jnp.float32), axis=0).astype(jnp.bfloat16)

    placed = jnp.where(slot_hot[:, :, None], down[:, None, :], jnp.zeros((), jnp.bfloat16))
    lift = jnp.dot(
        placed.reshape(row_count, holders * rank),
        up_w.reshape(holders * rank, out_width),
        preferred_element_type=jnp.float32,
    ).astype(jnp.bfloat16)
    return (base_total + lift.astype(jnp.float32)).astype(jnp.bfloat16)


def coordinate(device, c):
    return device.core_on_chip if c == 3 else device.coords[c]


def fine_mesh(mesh):
    parts = [split_axis(mesh, name) for name in mesh.axis_names]
    names = [tuple(f"{name}{c}" for c, _ in p) for name, p in zip(mesh.axis_names, parts)]
    flat = [q for p in parts for q in p]
    devices = mesh.devices.reshape([n for _, n in flat])
    for k, (c, n) in enumerate(flat):
        for index in np.ndindex(devices.shape):
            if index[k] + 1 < n:
                step = list(index)
                step[k] += 1
                a, b = devices[index], devices[tuple(step)]
                if any((coordinate(a, o) != coordinate(b, o)) != (o == c) for o in range(4)):
                    return mesh, tuple((name,) for name in mesh.axis_names)
    return Mesh(devices, tuple(q for p in names for q in p)), tuple(names)


def solution(mesh):
    global DP, MP
    fine, (DP, MP) = fine_mesh(mesh)
    placed = (
        P(DP, MP),
        P(MP, None),
        P(DP, None, MP),
        P(DP, None, MP),
        P(DP, None),
        P(),
    )
    return jax.shard_map(per_device, mesh=fine, in_specs=placed, out_specs=P(DP, MP), check_vma=False)
```

```python
import jax
import jax.numpy as jnp
import numpy as np
from jax import lax
from jax.sharding import Mesh, PartitionSpec as P


def spread_over(block, axis):
    n = lax.axis_size(axis)
    return lax.all_to_all(jnp.broadcast_to(block[None], (n,) + block.shape), axis, 0, 0, tiled=False)


def split_axis(mesh, name):
    lead = [slice(None) if a == name else 0 for a in mesh.axis_names]
    line = mesh.devices[tuple(lead)].reshape(-1)
    parts = []
    for c in range(3):
        n = len({d.coords[c] for d in line})
        if n > 1:
            parts.append((c, n))
    if len({d.core_on_chip for d in line}) > 1:
        parts.append((3, 2))
    return parts


def per_device(hidden_rows, base_weight, adapter_down, adapter_up, adapter_of_row, holder_map):
    row_count, feat_width = hidden_rows.shape
    holders = lax.axis_size(DP)
    n_mp = lax.axis_size(MP)
    rank = adapter_down.shape[1]
    out_width = adapter_up.shape[2]
    adapters = holder_map.shape[0]

    adapter_ids = adapter_of_row[:, 0]
    matches = adapter_ids[:, None] == jnp.arange(adapters, dtype=jnp.int32)[None, :]
    slot_of_row = jnp.sum(jnp.where(matches, holder_map[None, :], 0), axis=1)
    slot_hot = slot_of_row[:, None] == jnp.arange(holders, dtype=jnp.int32)[None, :]

    both = jnp.concatenate([adapter_down[0], adapter_up[0]], axis=1)[None]
    for axis in reversed(DP):
        if axis == DP[-1] and len(DP) > 1:
            both = lax.all_gather(both, axis, axis=0, tiled=False)
            first_stage = both
        else:
            both = spread_over(both, axis)
    stack = both.reshape(holders, rank, both.shape[-1])
    down_w = stack[:, :, :feat_width]
    up_w = stack[:, :, feat_width:]

    base_terms = jnp.dot(hidden_rows, base_weight, preferred_element_type=jnp.float32)
    base_bf = base_terms.astype(jnp.bfloat16)
    if len(DP) > 1:
        base_bf, first_stage = lax.optimization_barrier((base_bf, first_stage))
    total = base_bf.reshape(row_count, *[lax.axis_size(a) for a in MP], -1)
    for k in reversed(range(len(MP))):
        total = lax.all_to_all(total, MP[k], 1 + k, 1 + k, tiled=True)
        total = jnp.sum(total.astype(jnp.float32), axis=1 + k, keepdims=True)
        if k:
            total = total.astype(jnp.bfloat16)
    base_total = total.reshape(row_count, -1)

    every = jnp.dot(
        hidden_rows,
        down_w.transpose(2, 0, 1).reshape(feat_width, holders * rank),
        preferred_element_type=jnp.float32,
    ).reshape(row_count, holders, rank)
    partial_down = jnp.sum(jnp.where(slot_hot[:, :, None], every, 0.0), axis=1)
    gathered = partial_down.astype(jnp.bfloat16)[None]
    for axis in MP:
        gathered = spread_over(gathered, axis)
    gathered = gathered.reshape(n_mp, row_count, rank)
    down = jnp.sum(gathered.astype(jnp.float32), axis=0).astype(jnp.bfloat16)

    placed = jnp.where(slot_hot[:, :, None], down[:, None, :], jnp.zeros((), jnp.bfloat16))
    lift = jnp.dot(
        placed.reshape(row_count, holders * rank),
        up_w.reshape(holders * rank, out_width),
        preferred_element_type=jnp.float32,
    ).astype(jnp.bfloat16)
    return (base_total + lift.astype(jnp.float32)).astype(jnp.bfloat16)


def coordinate(device, c):
    return device.core_on_chip if c == 3 else device.coords[c]


def fine_mesh(mesh):
    parts = [split_axis(mesh, name) for name in mesh.axis_names]
    names = [tuple(f"{name}{c}" for c, _ in p) for name, p in zip(mesh.axis_names, parts)]
    flat = [q for p in parts for q in p]
    devices = mesh.devices.reshape([n for _, n in flat])
    for k, (c, n) in enumerate(flat):
        for index in np.ndindex(devices.shape):
            if index[k] + 1 < n:
                step = list(index)
                step[k] += 1
                a, b = devices[index], devices[tuple(step)]
                if any((coordinate(a, o) != coordinate(b, o)) != (o == c) for o in range(4)):
                    return mesh, tuple((name,) for name in mesh.axis_names)
    return Mesh(devices, tuple(q for p in names for q in p)), tuple(names)


def solution(mesh):
    global DP, MP
    fine, (DP, MP) = fine_mesh(mesh)
    placed = (
        P(DP, MP),
        P(MP, None),
        P(DP, None, MP),
        P(DP, None, MP),
        P(DP, None),
        P(),
    )
    return jax.shard_map(per_device, mesh=fine, in_specs=placed, out_specs=P(DP, MP), check_vma=False)
```

```python
import jax
import jax.numpy as jnp
import numpy as np
from jax import lax
from jax.sharding import Mesh, PartitionSpec as P


def spread_over(block, axis):
    n = lax.axis_size(axis)
    return lax.all_to_all(jnp.broadcast_to(block[None], (n,) + block.shape), axis, 0, 0, tiled=False)


def split_axis(mesh, name):
    lead = [slice(None) if a == name else 0 for a in mesh.axis_names]
    line = mesh.devices[tuple(lead)].reshape(-1)
    parts = []
    for c in range(3):
        n = len({d.coords[c] for d in line})
        if n > 1:
            parts.append((c, n))
    if len({d.core_on_chip for d in line}) > 1:
        parts.append((3, 2))
    return parts


def per_device(hidden_rows, base_weight, adapter_down, adapter_up, adapter_of_row, holder_map):
    row_count, feat_width = hidden_rows.shape
    holders = lax.axis_size(DP)
    n_mp = lax.axis_size(MP)
    rank = adapter_down.shape[1]
    out_width = adapter_up.shape[2]
    adapters = holder_map.shape[0]

    adapter_ids = adapter_of_row[:, 0]
    matches = adapter_ids[:, None] == jnp.arange(adapters, dtype=jnp.int32)[None, :]
    slot_of_row = jnp.sum(jnp.where(matches, holder_map[None, :], 0), axis=1)
    slot_hot = slot_of_row[:, None] == jnp.arange(holders, dtype=jnp.int32)[None, :]

    both = jnp.concatenate([adapter_down[0], adapter_up[0]], axis=1)[None]
    both = lax.all_gather(both, DP[-1], axis=0, tiled=False)
    down_w = both[..., :feat_width]
    up_w = both[..., feat_width:]
    for axis in reversed(DP[:-1]):
        down_w = spread_over(down_w, axis)
    down_w = down_w.reshape(holders, rank, feat_width)

    base_terms = jnp.dot(hidden_rows, base_weight, preferred_element_type=jnp.float32)
    base_bf = base_terms.astype(jnp.bfloat16)
    base_total = lax.psum_scatter(base_bf, MP, scatter_dimension=1, tiled=True).astype(
        jnp.float32
    )
    up_w, base_total = lax.optimization_barrier((up_w, base_total))
    for axis in reversed(DP[:-1]):
        up_w = lax.all_gather(up_w, axis, axis=0, tiled=False)
    up_w = up_w.reshape(holders, rank, out_width)

    every = jnp.dot(
        hidden_rows,
        down_w.transpose(2, 0, 1).reshape(feat_width, holders * rank),
        preferred_element_type=jnp.float32,
    ).reshape(row_count, holders, rank)
    partial_down = jnp.sum(jnp.where(slot_hot[:, :, None], every, 0.0), axis=1)
    gathered = partial_down.astype(jnp.bfloat16)[None]
    for axis in MP:
        gathered = spread_over(gathered, axis)
    gathered = gathered.reshape(n_mp, row_count, rank)
    down = jnp.sum(gathered.astype(jnp.float32), axis=0).astype(jnp.bfloat16)

    placed = jnp.where(slot_hot[:, :, None], down[:, None, :], jnp.zeros((), jnp.bfloat16))
    lift = jnp.dot(
        placed.reshape(row_count, holders * rank),
        up_w.reshape(holders * rank, out_width),
        preferred_element_type=jnp.float32,
    ).astype(jnp.bfloat16)
    return (base_total + lift.astype(jnp.float32)).astype(jnp.bfloat16)


def coordinate(device, c):
    return device.core_on_chip if c == 3 else device.coords[c]


def fine_mesh(mesh):
    parts = [split_axis(mesh, name) for name in mesh.axis_names]
    names = [tuple(f"{name}{c}" for c, _ in p) for name, p in zip(mesh.axis_names, parts)]
    flat = [q for p in parts for q in p]
    devices = mesh.devices.reshape([n for _, n in flat])
    for k, (c, n) in enumerate(flat):
        for index in np.ndindex(devices.shape):
            if index[k] + 1 < n:
                step = list(index)
                step[k] += 1
                a, b = devices[index], devices[tuple(step)]
                if any((coordinate(a, o) != coordinate(b, o)) != (o == c) for o in range(4)):
                    return mesh, tuple((name,) for name in mesh.axis_names)
    return Mesh(devices, tuple(q for p in names for q in p)), tuple(names)


def solution(mesh):
    global DP, MP
    fine, (DP, MP) = fine_mesh(mesh)
    placed = (
        P(DP, MP),
        P(MP, None),
        P(DP, None, MP),
        P(DP, None, MP),
        P(DP, None),
        P(),
    )
    return jax.shard_map(per_device, mesh=fine, in_specs=placed, out_specs=P(DP, MP), check_vma=False)
```

```python
import jax
import jax.numpy as jnp
import numpy as np
from jax import lax
from jax.sharding import Mesh, PartitionSpec as P


def spread_over(block, axis):
    n = lax.axis_size(axis)
    return lax.all_to_all(jnp.broadcast_to(block[None], (n,) + block.shape), axis, 0, 0, tiled=False)


def split_axis(mesh, name):
    lead = [slice(None) if a == name else 0 for a in mesh.axis_names]
    line = mesh.devices[tuple(lead)].reshape(-1)
    parts = []
    for c in range(3):
        n = len({d.coords[c] for d in line})
        if n > 1:
            parts.append((c, n))
    if len({d.core_on_chip for d in line}) > 1:
        parts.append((3, 2))
    return parts


def per_device(hidden_rows, base_weight, adapter_down, adapter_up, adapter_of_row, holder_map):
    row_count, feat_width = hidden_rows.shape
    holders = lax.axis_size(DP)
    n_mp = lax.axis_size(MP)
    rank = adapter_down.shape[1]
    out_width = adapter_up.shape[2]
    adapters = holder_map.shape[0]

    adapter_ids = adapter_of_row[:, 0]
    matches = adapter_ids[:, None] == jnp.arange(adapters, dtype=jnp.int32)[None, :]
    slot_of_row = jnp.sum(jnp.where(matches, holder_map[None, :], 0), axis=1)
    slot_hot = slot_of_row[:, None] == jnp.arange(holders, dtype=jnp.int32)[None, :]

    both = jnp.concatenate([adapter_down[0], adapter_up[0]], axis=1)[None]
    both = lax.all_gather(both, DP[-1], axis=0, tiled=False)
    down_w = both[..., :feat_width]
    up_w = both[..., feat_width:]
    for axis in reversed(DP[:-1]):
        down_w = spread_over(down_w, axis)
    down_w = down_w.reshape(holders, rank, feat_width)

    base_terms = jnp.dot(hidden_rows, base_weight, preferred_element_type=jnp.float32)
    base_bf = base_terms.astype(jnp.bfloat16)
    base_total = lax.psum_scatter(base_bf, MP, scatter_dimension=1, tiled=True).astype(
        jnp.float32
    )
    up_w, base_total = lax.optimization_barrier((up_w, base_total))
    for axis in reversed(DP[:-1]):
        up_w = lax.all_gather(up_w, axis, axis=0, tiled=False)
    up_w = up_w.reshape(holders, rank, out_width)

    every = jnp.dot(
        hidden_rows,
        down_w.transpose(2, 0, 1).reshape(feat_width, holders * rank),
        preferred_element_type=jnp.float32,
    ).reshape(row_count, holders, rank)
    partial_down = jnp.sum(jnp.where(slot_hot[:, :, None], every, 0.0), axis=1)
    gathered = partial_down.astype(jnp.bfloat16)[None]
    for axis in reversed(MP):
        gathered = spread_over(gathered, axis)
    gathered = gathered.reshape(n_mp, row_count, rank)
    down = jnp.sum(gathered.astype(jnp.float32), axis=0).astype(jnp.bfloat16)

    placed = jnp.where(slot_hot[:, :, None], down[:, None, :], jnp.zeros((), jnp.bfloat16))
    lift = jnp.dot(
        placed.reshape(row_count, holders * rank),
        up_w.reshape(holders * rank, out_width),
        preferred_element_type=jnp.float32,
    ).astype(jnp.bfloat16)
    return (base_total + lift.astype(jnp.float32)).astype(jnp.bfloat16)


def coordinate(device, c):
    return device.core_on_chip if c == 3 else device.coords[c]


def fine_mesh(mesh):
    parts = [split_axis(mesh, name) for name in mesh.axis_names]
    names = [tuple(f"{name}{c}" for c, _ in p) for name, p in zip(mesh.axis_names, parts)]
    flat = [q for p in parts for q in p]
    devices = mesh.devices.reshape([n for _, n in flat])
    for k, (c, n) in enumerate(flat):
        for index in np.ndindex(devices.shape):
            if index[k] + 1 < n:
                step = list(index)
                step[k] += 1
                a, b = devices[index], devices[tuple(step)]
                if any((coordinate(a, o) != coordinate(b, o)) != (o == c) for o in range(4)):
                    return mesh, tuple((name,) for name in mesh.axis_names)
    return Mesh(devices, tuple(q for p in names for q in p)), tuple(names)


def solution(mesh):
    global DP, MP
    fine, (DP, MP) = fine_mesh(mesh)
    placed = (
        P(DP, MP),
        P(MP, None),
        P(DP, None, MP),
        P(DP, None, MP),
        P(DP, None),
        P(),
    )
    return jax.shard_map(per_device, mesh=fine, in_specs=placed, out_specs=P(DP, MP), check_vma=False)
```

```python
import jax
import jax.numpy as jnp
import numpy as np
from jax import lax
from jax.experimental import pallas as pl
from jax.experimental.pallas import tpu as pltpu
from jax.sharding import Mesh, PartitionSpec as P


def spread_over(block, axis):
    n = lax.axis_size(axis)
    return lax.all_to_all(jnp.broadcast_to(block[None], (n,) + block.shape), axis, 0, 0, tiled=False)


def _product_block(x_ref, w_ref, o_ref):
    o_ref[...] = jnp.dot(x_ref[...], w_ref[...], preferred_element_type=jnp.float32).astype(
        o_ref.dtype
    )


def base_product(x, w, block=1024):
    rows, inner = x.shape
    cols = w.shape[1]
    block = block if cols % block == 0 else cols
    return pl.pallas_call(
        _product_block,
        grid=(cols // block,),
        in_specs=[
            pl.BlockSpec((rows, inner), lambda j: (0, 0)),
            pl.BlockSpec((inner, block), lambda j: (0, j)),
        ],
        out_specs=pl.BlockSpec((rows, block), lambda j: (0, j)),
        out_shape=jax.ShapeDtypeStruct((rows, cols), jnp.bfloat16),
        cost_estimate=pl.CostEstimate(
            flops=2 * rows * inner * cols,
            transcendentals=0,
            bytes_accessed=2 * (rows * inner + inner * cols + rows * cols),
        ),
    )(x, w)


def split_axis(mesh, name):
    lead = [slice(None) if a == name else 0 for a in mesh.axis_names]
    line = mesh.devices[tuple(lead)].reshape(-1)
    parts = []
    for c in range(3):
        n = len({d.coords[c] for d in line})
        if n > 1:
            parts.append((c, n))
    if len({d.core_on_chip for d in line}) > 1:
        parts.append((3, 2))
    return parts


def per_device(hidden_rows, base_weight, adapter_down, adapter_up, adapter_of_row, holder_map):
    row_count, feat_width = hidden_rows.shape
    holders = lax.axis_size(DP)
    n_mp = lax.axis_size(MP)
    rank = adapter_down.shape[1]
    out_width = adapter_up.shape[2]
    adapters = holder_map.shape[0]

    adapter_ids = adapter_of_row[:, 0]
    matches = adapter_ids[:, None] == jnp.arange(adapters, dtype=jnp.int32)[None, :]
    slot_of_row = jnp.sum(jnp.where(matches, holder_map[None, :], 0), axis=1)
    slot_hot = slot_of_row[:, None] == jnp.arange(holders, dtype=jnp.int32)[None, :]

    both = jnp.concatenate([adapter_down[0], adapter_up[0]], axis=1)[None]
    both = lax.all_gather(both, DP[-1], axis=0, tiled=False)
    down_w = both[..., :feat_width]
    up_w = both[..., feat_width:]
    for axis in reversed(DP[:-1]):
        down_w = spread_over(down_w, axis)
    down_w = down_w.reshape(holders, rank, feat_width)

    base_bf = base_product(hidden_rows, base_weight)
    base_total = lax.psum_scatter(base_bf, MP, scatter_dimension=1, tiled=True).astype(
        jnp.float32
    )
    up_w, base_total = lax.optimization_barrier((up_w, base_total))
    for axis in reversed(DP[:-1]):
        up_w = lax.all_gather(up_w, axis, axis=0, tiled=False)
    up_w = up_w.reshape(holders, rank, out_width)

    every = jnp.dot(
        hidden_rows,
        down_w.transpose(2, 0, 1).reshape(feat_width, holders * rank),
        preferred_element_type=jnp.float32,
    ).reshape(row_count, holders, rank)
    partial_down = jnp.sum(jnp.where(slot_hot[:, :, None], every, 0.0), axis=1)
    gathered = partial_down.astype(jnp.bfloat16)[None]
    for axis in MP:
        gathered = spread_over(gathered, axis)
    gathered = gathered.reshape(n_mp, row_count, rank)
    down = jnp.sum(gathered.astype(jnp.float32), axis=0).astype(jnp.bfloat16)

    placed = jnp.where(slot_hot[:, :, None], down[:, None, :], jnp.zeros((), jnp.bfloat16))
    lift = jnp.dot(
        placed.reshape(row_count, holders * rank),
        up_w.reshape(holders * rank, out_width),
        preferred_element_type=jnp.float32,
    ).astype(jnp.bfloat16)
    return (base_total + lift.astype(jnp.float32)).astype(jnp.bfloat16)


def coordinate(device, c):
    return device.core_on_chip if c == 3 else device.coords[c]


def fine_mesh(mesh):
    parts = [split_axis(mesh, name) for name in mesh.axis_names]
    names = [tuple(f"{name}{c}" for c, _ in p) for name, p in zip(mesh.axis_names, parts)]
    flat = [q for p in parts for q in p]
    devices = mesh.devices.reshape([n for _, n in flat])
    for k, (c, n) in enumerate(flat):
        for index in np.ndindex(devices.shape):
            if index[k] + 1 < n:
                step = list(index)
                step[k] += 1
                a, b = devices[index], devices[tuple(step)]
                if any((coordinate(a, o) != coordinate(b, o)) != (o == c) for o in range(4)):
                    return mesh, tuple((name,) for name in mesh.axis_names)
    return Mesh(devices, tuple(q for p in names for q in p)), tuple(names)


def solution(mesh):
    global DP, MP
    fine, (DP, MP) = fine_mesh(mesh)
    placed = (
        P(DP, MP),
        P(MP, None),
        P(DP, None, MP),
        P(DP, None, MP),
        P(DP, None),
        P(),
    )
    return jax.shard_map(per_device, mesh=fine, in_specs=placed, out_specs=P(DP, MP), check_vma=False)
```

```python
import jax
import jax.numpy as jnp
import numpy as np
from jax import lax
from jax.experimental import pallas as pl
from jax.experimental.pallas import tpu as pltpu
from jax.sharding import Mesh, PartitionSpec as P


def spread_over(block, axis):
    n = lax.axis_size(axis)
    return lax.all_to_all(jnp.broadcast_to(block[None], (n,) + block.shape), axis, 0, 0, tiled=False)


def _product_block(x_ref, w_ref, o_ref):
    o_ref[...] = jnp.dot(x_ref[...], w_ref[...], preferred_element_type=jnp.float32).astype(
        o_ref.dtype
    )


def base_product(x, w, block=1024):
    rows, inner = x.shape
    cols = w.shape[1]
    block = block if cols % block == 0 else cols
    return pl.pallas_call(
        _product_block,
        grid=(cols // block,),
        in_specs=[
            pl.BlockSpec((rows, inner), lambda j: (0, 0)),
            pl.BlockSpec((inner, block), lambda j: (0, j)),
        ],
        out_specs=pl.BlockSpec((rows, block), lambda j: (0, j)),
        out_shape=jax.ShapeDtypeStruct((rows, cols), jnp.bfloat16),
        cost_estimate=pl.CostEstimate(
            flops=2 * rows * inner * cols,
            transcendentals=0,
            bytes_accessed=2 * (rows * inner + inner * cols + rows * cols),
        ),
    )(x, w)


def split_axis(mesh, name):
    lead = [slice(None) if a == name else 0 for a in mesh.axis_names]
    line = mesh.devices[tuple(lead)].reshape(-1)
    parts = []
    for c in range(3):
        n = len({d.coords[c] for d in line})
        if n > 1:
            parts.append((c, n))
    if len({d.core_on_chip for d in line}) > 1:
        parts.append((3, 2))
    return parts


def per_device(hidden_rows, base_weight, adapter_down, adapter_up, adapter_of_row, holder_map):
    row_count, feat_width = hidden_rows.shape
    holders = lax.axis_size(DP)
    n_mp = lax.axis_size(MP)
    rank = adapter_down.shape[1]
    out_width = adapter_up.shape[2]
    adapters = holder_map.shape[0]

    adapter_ids = adapter_of_row[:, 0]
    matches = adapter_ids[:, None] == jnp.arange(adapters, dtype=jnp.int32)[None, :]
    slot_of_row = jnp.sum(jnp.where(matches, holder_map[None, :], 0), axis=1)
    slot_hot = slot_of_row[:, None] == jnp.arange(holders, dtype=jnp.int32)[None, :]

    both = jnp.concatenate([adapter_down[0], adapter_up[0]], axis=1)[None]
    both = lax.all_gather(both, DP[-1], axis=0, tiled=False)
    down_w = both[..., :feat_width]
    up_w = both[..., feat_width:]
    for axis in reversed(DP[:-1]):
        down_w = spread_over(down_w, axis)
    down_w = down_w.reshape(holders, rank, feat_width)

    base_t = lax.dot_general(
        base_weight, hidden_rows, (((0,), (1,)), ((), ())), preferred_element_type=jnp.float32
    ).astype(jnp.bfloat16)
    base_total = lax.psum_scatter(base_t, MP, scatter_dimension=0, tiled=True).astype(jnp.float32)
    up_w, base_total = lax.optimization_barrier((up_w, base_total))
    for axis in reversed(DP[:-1]):
        up_w = lax.all_gather(up_w, axis, axis=0, tiled=False)
    up_w = up_w.reshape(holders, rank, out_width)

    every = jnp.dot(
        hidden_rows,
        down_w.transpose(2, 0, 1).reshape(feat_width, holders * rank),
        preferred_element_type=jnp.float32,
    ).reshape(row_count, holders, rank)
    partial_down = jnp.sum(jnp.where(slot_hot[:, :, None], every, 0.0), axis=1)
    gathered = partial_down.astype(jnp.bfloat16)[None]
    for axis in MP:
        gathered = spread_over(gathered, axis)
    gathered = gathered.reshape(n_mp, row_count, rank)
    down = jnp.sum(gathered.astype(jnp.float32), axis=0).astype(jnp.bfloat16)

    placed = jnp.where(slot_hot[:, :, None], down[:, None, :], jnp.zeros((), jnp.bfloat16))
    lift = jnp.dot(
        placed.reshape(row_count, holders * rank),
        up_w.reshape(holders * rank, out_width),
        preferred_element_type=jnp.float32,
    ).astype(jnp.bfloat16)
    return (base_total.T + lift.astype(jnp.float32)).astype(jnp.bfloat16)


def coordinate(device, c):
    return device.core_on_chip if c == 3 else device.coords[c]


def fine_mesh(mesh):
    parts = [split_axis(mesh, name) for name in mesh.axis_names]
    names = [tuple(f"{name}{c}" for c, _ in p) for name, p in zip(mesh.axis_names, parts)]
    flat = [q for p in parts for q in p]
    devices = mesh.devices.reshape([n for _, n in flat])
    for k, (c, n) in enumerate(flat):
        for index in np.ndindex(devices.shape):
            if index[k] + 1 < n:
                step = list(index)
                step[k] += 1
                a, b = devices[index], devices[tuple(step)]
                if any((coordinate(a, o) != coordinate(b, o)) != (o == c) for o in range(4)):
                    return mesh, tuple((name,) for name in mesh.axis_names)
    return Mesh(devices, tuple(q for p in names for q in p)), tuple(names)


def solution(mesh):
    global DP, MP
    fine, (DP, MP) = fine_mesh(mesh)
    placed = (
        P(DP, MP),
        P(MP, None),
        P(DP, None, MP),
        P(DP, None, MP),
        P(DP, None),
        P(),
    )
    return jax.shard_map(per_device, mesh=fine, in_specs=placed, out_specs=P(DP, MP), check_vma=False)
```

```python
import jax
import jax.numpy as jnp
import numpy as np
from jax import lax
from jax.experimental import pallas as pl
from jax.experimental.pallas import tpu as pltpu
from jax.sharding import Mesh, PartitionSpec as P


def spread_over(block, axis):
    n = lax.axis_size(axis)
    return lax.all_to_all(jnp.broadcast_to(block[None], (n,) + block.shape), axis, 0, 0, tiled=False)


def _product_block(x_ref, w_ref, o_ref):
    o_ref[...] = jnp.dot(x_ref[...], w_ref[...], preferred_element_type=jnp.float32).astype(
        o_ref.dtype
    )


def base_product(x, w, block=1024):
    rows, inner = x.shape
    cols = w.shape[1]
    block = block if cols % block == 0 else cols
    return pl.pallas_call(
        _product_block,
        grid=(cols // block,),
        in_specs=[
            pl.BlockSpec((rows, inner), lambda j: (0, 0)),
            pl.BlockSpec((inner, block), lambda j: (0, j)),
        ],
        out_specs=pl.BlockSpec((rows, block), lambda j: (0, j)),
        out_shape=jax.ShapeDtypeStruct((rows, cols), jnp.bfloat16),
        cost_estimate=pl.CostEstimate(
            flops=2 * rows * inner * cols,
            transcendentals=0,
            bytes_accessed=2 * (rows * inner + inner * cols + rows * cols),
        ),
    )(x, w)


def split_axis(mesh, name):
    lead = [slice(None) if a == name else 0 for a in mesh.axis_names]
    line = mesh.devices[tuple(lead)].reshape(-1)
    parts = []
    for c in range(3):
        n = len({d.coords[c] for d in line})
        if n > 1:
            parts.append((c, n))
    if len({d.core_on_chip for d in line}) > 1:
        parts.append((3, 2))
    return parts


def per_device(hidden_rows, base_weight, adapter_down, adapter_up, adapter_of_row, holder_map):
    row_count, feat_width = hidden_rows.shape
    holders = lax.axis_size(DP)
    n_mp = lax.axis_size(MP)
    rank = adapter_down.shape[1]
    out_width = adapter_up.shape[2]
    adapters = holder_map.shape[0]

    adapter_ids = adapter_of_row[:, 0]
    matches = adapter_ids[:, None] == jnp.arange(adapters, dtype=jnp.int32)[None, :]
    slot_of_row = jnp.sum(jnp.where(matches, holder_map[None, :], 0), axis=1)
    slot_hot = slot_of_row[:, None] == jnp.arange(holders, dtype=jnp.int32)[None, :]

    both = jnp.concatenate([adapter_down[0], adapter_up[0]], axis=1)[None]
    both = lax.all_gather(both, DP[-1], axis=0, tiled=False)
    down_w = both[..., :feat_width]
    up_w = both[..., feat_width:]
    for axis in reversed(DP[:-1]):
        down_w = spread_over(down_w, axis)
    down_w = down_w.reshape(holders, rank, feat_width)

    if len(MP) == 2:
        n_y, n_c = lax.axis_size(MP[0]), lax.axis_size(MP[1])
        base_t = lax.dot_general(
            base_weight.reshape(feat_width, n_y, n_c, -1),
            hidden_rows,
            (((0,), (1,)), ((), ())),
            preferred_element_type=jnp.float32,
        ).astype(jnp.bfloat16)
        base_t = base_t.transpose(1, 0, 2, 3)
        base_t = lax.all_to_all(base_t, MP[1], 0, 0, tiled=True)
        base_t = jnp.sum(base_t.astype(jnp.float32), axis=0).astype(jnp.bfloat16)
        base_t = lax.psum_scatter(base_t, MP[0], scatter_dimension=0, tiled=True)
        base_total = base_t.reshape(-1, row_count).T.astype(jnp.float32)
    else:
        base_bf = base_product(hidden_rows, base_weight)
        base_total = lax.psum_scatter(base_bf, MP, scatter_dimension=1, tiled=True).astype(
            jnp.float32
        )
    up_w, base_total = lax.optimization_barrier((up_w, base_total))
    for axis in reversed(DP[:-1]):
        up_w = lax.all_gather(up_w, axis, axis=0, tiled=False)
    up_w = up_w.reshape(holders, rank, out_width)

    every = jnp.dot(
        hidden_rows,
        down_w.transpose(2, 0, 1).reshape(feat_width, holders * rank),
        preferred_element_type=jnp.float32,
    ).reshape(row_count, holders, rank)
    partial_down = jnp.sum(jnp.where(slot_hot[:, :, None], every, 0.0), axis=1)
    gathered = partial_down.astype(jnp.bfloat16)[None]
    for axis in MP:
        gathered = spread_over(gathered, axis)
    gathered = gathered.reshape(n_mp, row_count, rank)
    down = jnp.sum(gathered.astype(jnp.float32), axis=0).astype(jnp.bfloat16)

    placed = jnp.where(slot_hot[:, :, None], down[:, None, :], jnp.zeros((), jnp.bfloat16))
    lift = jnp.dot(
        placed.reshape(row_count, holders * rank),
        up_w.reshape(holders * rank, out_width),
        preferred_element_type=jnp.float32,
    ).astype(jnp.bfloat16)
    return (base_total + lift.astype(jnp.float32)).astype(jnp.bfloat16)


def coordinate(device, c):
    return device.core_on_chip if c == 3 else device.coords[c]


def fine_mesh(mesh):
    parts = [split_axis(mesh, name) for name in mesh.axis_names]
    names = [tuple(f"{name}{c}" for c, _ in p) for name, p in zip(mesh.axis_names, parts)]
    flat = [q for p in parts for q in p]
    devices = mesh.devices.reshape([n for _, n in flat])
    for k, (c, n) in enumerate(flat):
        for index in np.ndindex(devices.shape):
            if index[k] + 1 < n:
                step = list(index)
                step[k] += 1
                a, b = devices[index], devices[tuple(step)]
                if any((coordinate(a, o) != coordinate(b, o)) != (o == c) for o in range(4)):
                    return mesh, tuple((name,) for name in mesh.axis_names)
    return Mesh(devices, tuple(q for p in names for q in p)), tuple(names)


def solution(mesh):
    global DP, MP
    fine, (DP, MP) = fine_mesh(mesh)
    placed = (
        P(DP, MP),
        P(MP, None),
        P(DP, None, MP),
        P(DP, None, MP),
        P(DP, None),
        P(),
    )
    return jax.shard_map(per_device, mesh=fine, in_specs=placed, out_specs=P(DP, MP), check_vma=False)
```

```python
import jax
import jax.numpy as jnp
import numpy as np
from jax import lax
from jax.experimental import pallas as pl
from jax.experimental.pallas import tpu as pltpu
from jax.sharding import Mesh, PartitionSpec as P


def spread_over(block, axis):
    n = lax.axis_size(axis)
    return lax.all_to_all(jnp.broadcast_to(block[None], (n,) + block.shape), axis, 0, 0, tiled=False)


def _product_block(x_ref, w_ref, o_ref):
    o_ref[...] = jnp.dot(x_ref[...], w_ref[...], preferred_element_type=jnp.float32).astype(
        o_ref.dtype
    )


def base_product(x, w, block=1024):
    rows, inner = x.shape
    cols = w.shape[1]
    block = block if cols % block == 0 else cols
    return pl.pallas_call(
        _product_block,
        grid=(cols // block,),
        in_specs=[
            pl.BlockSpec((rows, inner), lambda j: (0, 0)),
            pl.BlockSpec((inner, block), lambda j: (0, j)),
        ],
        out_specs=pl.BlockSpec((rows, block), lambda j: (0, j)),
        out_shape=jax.ShapeDtypeStruct((rows, cols), jnp.bfloat16),
        cost_estimate=pl.CostEstimate(
            flops=2 * rows * inner * cols,
            transcendentals=0,
            bytes_accessed=2 * (rows * inner + inner * cols + rows * cols),
        ),
    )(x, w)


def split_axis(mesh, name):
    lead = [slice(None) if a == name else 0 for a in mesh.axis_names]
    line = mesh.devices[tuple(lead)].reshape(-1)
    parts = []
    for c in range(3):
        n = len({d.coords[c] for d in line})
        if n > 1:
            parts.append((c, n))
    if len({d.core_on_chip for d in line}) > 1:
        parts.append((3, 2))
    return parts


def per_device(hidden_rows, base_weight, adapter_down, adapter_up, adapter_of_row, holder_map):
    row_count, feat_width = hidden_rows.shape
    holders = lax.axis_size(DP)
    n_mp = lax.axis_size(MP)
    rank = adapter_down.shape[1]
    out_width = adapter_up.shape[2]
    adapters = holder_map.shape[0]

    adapter_ids = adapter_of_row[:, 0]
    matches = adapter_ids[:, None] == jnp.arange(adapters, dtype=jnp.int32)[None, :]
    slot_of_row = jnp.sum(jnp.where(matches, holder_map[None, :], 0), axis=1)
    slot_hot = slot_of_row[:, None] == jnp.arange(holders, dtype=jnp.int32)[None, :]

    both = jnp.concatenate([adapter_down[0], adapter_up[0]], axis=1)[None]
    both = lax.all_gather(both, DP[-1], axis=0, tiled=False)
    down_w = both[..., :feat_width]
    up_w = both[..., feat_width:]
    for axis in reversed(DP[:-1]):
        down_w = spread_over(down_w, axis)
    down_w = down_w.reshape(holders, rank, feat_width)

    base_bf = base_product(hidden_rows, base_weight)
    base_total = lax.psum_scatter(base_bf, MP, scatter_dimension=1, tiled=True)
    up_w, base_total = lax.optimization_barrier((up_w, base_total))
    base_total = base_total.astype(jnp.float32)
    for axis in reversed(DP[:-1]):
        up_w = lax.all_gather(up_w, axis, axis=0, tiled=False)
    up_w = up_w.reshape(holders, rank, out_width)

    every = jnp.dot(
        hidden_rows,
        down_w.transpose(2, 0, 1).reshape(feat_width, holders * rank),
        preferred_element_type=jnp.float32,
    ).reshape(row_count, holders, rank)
    partial_down = jnp.sum(jnp.where(slot_hot[:, :, None], every, 0.0), axis=1)
    gathered = partial_down.astype(jnp.bfloat16)[None]
    for axis in MP:
        gathered = spread_over(gathered, axis)
    gathered = gathered.reshape(n_mp, row_count, rank)
    down = jnp.sum(gathered.astype(jnp.float32), axis=0).astype(jnp.bfloat16)

    placed = jnp.where(slot_hot[:, :, None], down[:, None, :], jnp.zeros((), jnp.bfloat16))
    lift = jnp.dot(
        placed.reshape(row_count, holders * rank),
        up_w.reshape(holders * rank, out_width),
        preferred_element_type=jnp.float32,
    ).astype(jnp.bfloat16)
    return (base_total + lift.astype(jnp.float32)).astype(jnp.bfloat16)


def coordinate(device, c):
    return device.core_on_chip if c == 3 else device.coords[c]


def fine_mesh(mesh):
    parts = [split_axis(mesh, name) for name in mesh.axis_names]
    names = [tuple(f"{name}{c}" for c, _ in p) for name, p in zip(mesh.axis_names, parts)]
    flat = [q for p in parts for q in p]
    devices = mesh.devices.reshape([n for _, n in flat])
    for k, (c, n) in enumerate(flat):
        for index in np.ndindex(devices.shape):
            if index[k] + 1 < n:
                step = list(index)
                step[k] += 1
                a, b = devices[index], devices[tuple(step)]
                if any((coordinate(a, o) != coordinate(b, o)) != (o == c) for o in range(4)):
                    return mesh, tuple((name,) for name in mesh.axis_names)
    return Mesh(devices, tuple(q for p in names for q in p)), tuple(names)


def solution(mesh):
    global DP, MP
    fine, (DP, MP) = fine_mesh(mesh)
    placed = (
        P(DP, MP),
        P(MP, None),
        P(DP, None, MP),
        P(DP, None, MP),
        P(DP, None),
        P(),
    )
    return jax.shard_map(per_device, mesh=fine, in_specs=placed, out_specs=P(DP, MP), check_vma=False)
```

```python
import jax
import jax.numpy as jnp
import numpy as np
from jax import lax
from jax.experimental import pallas as pl
from jax.experimental.pallas import tpu as pltpu
from jax.sharding import Mesh, PartitionSpec as P


def spread_over(block, axis):
    n = lax.axis_size(axis)
    return lax.all_to_all(jnp.broadcast_to(block[None], (n,) + block.shape), axis, 0, 0, tiled=False)


def _product_block(x_ref, w_ref, o_ref):
    o_ref[...] = jnp.dot(x_ref[...], w_ref[...], preferred_element_type=jnp.float32).astype(
        o_ref.dtype
    )


def base_product(x, w, block=512):
    rows, inner = x.shape
    cols = w.shape[1]
    block = block if cols % block == 0 else cols
    return pl.pallas_call(
        _product_block,
        grid=(cols // block,),
        in_specs=[
            pl.BlockSpec((rows, inner), lambda j: (0, 0)),
            pl.BlockSpec((inner, block), lambda j: (0, j)),
        ],
        out_specs=pl.BlockSpec((rows, block), lambda j: (0, j)),
        out_shape=jax.ShapeDtypeStruct((rows, cols), jnp.bfloat16),
        cost_estimate=pl.CostEstimate(
            flops=2 * rows * inner * cols,
            transcendentals=0,
            bytes_accessed=2 * (rows * inner + inner * cols + rows * cols),
        ),
    )(x, w)


def split_axis(mesh, name):
    lead = [slice(None) if a == name else 0 for a in mesh.axis_names]
    line = mesh.devices[tuple(lead)].reshape(-1)
    parts = []
    for c in range(3):
        n = len({d.coords[c] for d in line})
        if n > 1:
            parts.append((c, n))
    if len({d.core_on_chip for d in line}) > 1:
        parts.append((3, 2))
    return parts


def per_device(hidden_rows, base_weight, adapter_down, adapter_up, adapter_of_row, holder_map):
    row_count, feat_width = hidden_rows.shape
    holders = lax.axis_size(DP)
    n_mp = lax.axis_size(MP)
    rank = adapter_down.shape[1]
    out_width = adapter_up.shape[2]
    adapters = holder_map.shape[0]

    adapter_ids = adapter_of_row[:, 0]
    matches = adapter_ids[:, None] == jnp.arange(adapters, dtype=jnp.int32)[None, :]
    slot_of_row = jnp.sum(jnp.where(matches, holder_map[None, :], 0), axis=1)
    slot_hot = slot_of_row[:, None] == jnp.arange(holders, dtype=jnp.int32)[None, :]

    both = jnp.concatenate([adapter_down[0], adapter_up[0]], axis=1)[None]
    both = lax.all_gather(both, DP[-1], axis=0, tiled=False)
    down_w = both[..., :feat_width]
    up_w = both[..., feat_width:]
    for axis in reversed(DP[:-1]):
        down_w = spread_over(down_w, axis)
    down_w = down_w.reshape(holders, rank, feat_width)

    base_bf = base_product(hidden_rows, base_weight)
    base_total = lax.psum_scatter(base_bf, MP, scatter_dimension=1, tiled=True).astype(
        jnp.float32
    )
    up_w, base_total = lax.optimization_barrier((up_w, base_total))
    for axis in reversed(DP[:-1]):
        up_w = lax.all_gather(up_w, axis, axis=0, tiled=False)
    up_w = up_w.reshape(holders, rank, out_width)

    every = jnp.dot(
        hidden_rows,
        down_w.transpose(2, 0, 1).reshape(feat_width, holders * rank),
        preferred_element_type=jnp.float32,
    ).reshape(row_count, holders, rank)
    partial_down = jnp.sum(jnp.where(slot_hot[:, :, None], every, 0.0), axis=1)
    gathered = partial_down.astype(jnp.bfloat16)[None]
    for axis in MP:
        gathered = spread_over(gathered, axis)
    gathered = gathered.reshape(n_mp, row_count, rank)
    down = jnp.sum(gathered.astype(jnp.float32), axis=0).astype(jnp.bfloat16)

    placed = jnp.where(slot_hot[:, :, None], down[:, None, :], jnp.zeros((), jnp.bfloat16))
    lift = jnp.dot(
        placed.reshape(row_count, holders * rank),
        up_w.reshape(holders * rank, out_width),
        preferred_element_type=jnp.float32,
    ).astype(jnp.bfloat16)
    return (base_total + lift.astype(jnp.float32)).astype(jnp.bfloat16)


def coordinate(device, c):
    return device.core_on_chip if c == 3 else device.coords[c]


def fine_mesh(mesh):
    parts = [split_axis(mesh, name) for name in mesh.axis_names]
    names = [tuple(f"{name}{c}" for c, _ in p) for name, p in zip(mesh.axis_names, parts)]
    flat = [q for p in parts for q in p]
    devices = mesh.devices.reshape([n for _, n in flat])
    for k, (c, n) in enumerate(flat):
        for index in np.ndindex(devices.shape):
            if index[k] + 1 < n:
                step = list(index)
                step[k] += 1
                a, b = devices[index], devices[tuple(step)]
                if any((coordinate(a, o) != coordinate(b, o)) != (o == c) for o in range(4)):
                    return mesh, tuple((name,) for name in mesh.axis_names)
    return Mesh(devices, tuple(q for p in names for q in p)), tuple(names)


def solution(mesh):
    global DP, MP
    fine, (DP, MP) = fine_mesh(mesh)
    placed = (
        P(DP, MP),
        P(MP, None),
        P(DP, None, MP),
        P(DP, None, MP),
        P(DP, None),
        P(),
    )
    return jax.shard_map(per_device, mesh=fine, in_specs=placed, out_specs=P(DP, MP), check_vma=False)
```

```python
import jax
import jax.numpy as jnp
import numpy as np
from jax import lax
from jax.experimental import pallas as pl
from jax.experimental.pallas import tpu as pltpu
from jax.sharding import Mesh, PartitionSpec as P


def spread_over(block, axis):
    n = lax.axis_size(axis)
    return lax.all_to_all(jnp.broadcast_to(block[None], (n,) + block.shape), axis, 0, 0, tiled=False)


def _product_block(x_ref, w_ref, o_ref):
    o_ref[...] = jnp.dot(x_ref[...], w_ref[...], preferred_element_type=jnp.float32).astype(
        o_ref.dtype
    )


def base_product(x, w, block=2048):
    rows, inner = x.shape
    cols = w.shape[1]
    block = block if cols % block == 0 else cols
    return pl.pallas_call(
        _product_block,
        grid=(cols // block,),
        in_specs=[
            pl.BlockSpec((rows, inner), lambda j: (0, 0)),
            pl.BlockSpec((inner, block), lambda j: (0, j)),
        ],
        out_specs=pl.BlockSpec((rows, block), lambda j: (0, j)),
        out_shape=jax.ShapeDtypeStruct((rows, cols), jnp.bfloat16),
        cost_estimate=pl.CostEstimate(
            flops=2 * rows * inner * cols,
            transcendentals=0,
            bytes_accessed=2 * (rows * inner + inner * cols + rows * cols),
        ),
    )(x, w)


def split_axis(mesh, name):
    lead = [slice(None) if a == name else 0 for a in mesh.axis_names]
    line = mesh.devices[tuple(lead)].reshape(-1)
    parts = []
    for c in range(3):
        n = len({d.coords[c] for d in line})
        if n > 1:
            parts.append((c, n))
    if len({d.core_on_chip for d in line}) > 1:
        parts.append((3, 2))
    return parts


def per_device(hidden_rows, base_weight, adapter_down, adapter_up, adapter_of_row, holder_map):
    row_count, feat_width = hidden_rows.shape
    holders = lax.axis_size(DP)
    n_mp = lax.axis_size(MP)
    rank = adapter_down.shape[1]
    out_width = adapter_up.shape[2]
    adapters = holder_map.shape[0]

    adapter_ids = adapter_of_row[:, 0]
    matches = adapter_ids[:, None] == jnp.arange(adapters, dtype=jnp.int32)[None, :]
    slot_of_row = jnp.sum(jnp.where(matches, holder_map[None, :], 0), axis=1)
    slot_hot = slot_of_row[:, None] == jnp.arange(holders, dtype=jnp.int32)[None, :]

    both = jnp.concatenate([adapter_down[0], adapter_up[0]], axis=1)[None]
    both = lax.all_gather(both, DP[-1], axis=0, tiled=False)
    down_w = both[..., :feat_width]
    up_w = both[..., feat_width:]
    for axis in reversed(DP[:-1]):
        down_w = spread_over(down_w, axis)
    down_w = down_w.reshape(holders, rank, feat_width)

    base_bf = base_product(hidden_rows, base_weight)
    base_total = lax.psum_scatter(base_bf, MP, scatter_dimension=1, tiled=True).astype(
        jnp.float32
    )
    up_w, base_total = lax.optimization_barrier((up_w, base_total))
    for axis in reversed(DP[:-1]):
        up_w = lax.all_gather(up_w, axis, axis=0, tiled=False)
    up_w = up_w.reshape(holders, rank, out_width)

    every = jnp.dot(
        hidden_rows,
        down_w.transpose(2, 0, 1).reshape(feat_width, holders * rank),
        preferred_element_type=jnp.float32,
    ).reshape(row_count, holders, rank)
    partial_down = jnp.sum(jnp.where(slot_hot[:, :, None], every, 0.0), axis=1)
    gathered = partial_down.astype(jnp.bfloat16)[None]
    for axis in MP:
        gathered = spread_over(gathered, axis)
    gathered = gathered.reshape(n_mp, row_count, rank)
    down = jnp.sum(gathered.astype(jnp.float32), axis=0).astype(jnp.bfloat16)

    placed = jnp.where(slot_hot[:, :, None], down[:, None, :], jnp.zeros((), jnp.bfloat16))
    lift = jnp.dot(
        placed.reshape(row_count, holders * rank),
        up_w.reshape(holders * rank, out_width),
        preferred_element_type=jnp.float32,
    ).astype(jnp.bfloat16)
    return (base_total + lift.astype(jnp.float32)).astype(jnp.bfloat16)


def coordinate(device, c):
    return device.core_on_chip if c == 3 else device.coords[c]


def fine_mesh(mesh):
    parts = [split_axis(mesh, name) for name in mesh.axis_names]
    names = [tuple(f"{name}{c}" for c, _ in p) for name, p in zip(mesh.axis_names, parts)]
    flat = [q for p in parts for q in p]
    devices = mesh.devices.reshape([n for _, n in flat])
    for k, (c, n) in enumerate(flat):
        for index in np.ndindex(devices.shape):
            if index[k] + 1 < n:
                step = list(index)
                step[k] += 1
                a, b = devices[index], devices[tuple(step)]
                if any((coordinate(a, o) != coordinate(b, o)) != (o == c) for o in range(4)):
                    return mesh, tuple((name,) for name in mesh.axis_names)
    return Mesh(devices, tuple(q for p in names for q in p)), tuple(names)


def solution(mesh):
    global DP, MP
    fine, (DP, MP) = fine_mesh(mesh)
    placed = (
        P(DP, MP),
        P(MP, None),
        P(DP, None, MP),
        P(DP, None, MP),
        P(DP, None),
        P(),
    )
    return jax.shard_map(per_device, mesh=fine, in_specs=placed, out_specs=P(DP, MP), check_vma=False)
```

```python
import jax
import jax.numpy as jnp
import numpy as np
from jax import lax
from jax.experimental import pallas as pl
from jax.experimental.pallas import tpu as pltpu
from jax.sharding import Mesh, PartitionSpec as P


def spread_over(block, axis):
    n = lax.axis_size(axis)
    return lax.all_to_all(jnp.broadcast_to(block[None], (n,) + block.shape), axis, 0, 0, tiled=False)


def _product_block(x_ref, w_ref, o_ref):
    o_ref[...] = jnp.dot(x_ref[...], w_ref[...], preferred_element_type=jnp.float32).astype(
        o_ref.dtype
    )


def base_product(x, w, block=4096):
    rows, inner = x.shape
    cols = w.shape[1]
    block = block if cols % block == 0 else cols
    return pl.pallas_call(
        _product_block,
        grid=(cols // block,),
        in_specs=[
            pl.BlockSpec((rows, inner), lambda j: (0, 0)),
            pl.BlockSpec((inner, block), lambda j: (0, j)),
        ],
        out_specs=pl.BlockSpec((rows, block), lambda j: (0, j)),
        out_shape=jax.ShapeDtypeStruct((rows, cols), jnp.bfloat16),
        cost_estimate=pl.CostEstimate(
            flops=2 * rows * inner * cols,
            transcendentals=0,
            bytes_accessed=2 * (rows * inner + inner * cols + rows * cols),
        ),
    )(x, w)


def split_axis(mesh, name):
    lead = [slice(None) if a == name else 0 for a in mesh.axis_names]
    line = mesh.devices[tuple(lead)].reshape(-1)
    parts = []
    for c in range(3):
        n = len({d.coords[c] for d in line})
        if n > 1:
            parts.append((c, n))
    if len({d.core_on_chip for d in line}) > 1:
        parts.append((3, 2))
    return parts


def per_device(hidden_rows, base_weight, adapter_down, adapter_up, adapter_of_row, holder_map):
    row_count, feat_width = hidden_rows.shape
    holders = lax.axis_size(DP)
    n_mp = lax.axis_size(MP)
    rank = adapter_down.shape[1]
    out_width = adapter_up.shape[2]
    adapters = holder_map.shape[0]

    adapter_ids = adapter_of_row[:, 0]
    matches = adapter_ids[:, None] == jnp.arange(adapters, dtype=jnp.int32)[None, :]
    slot_of_row = jnp.sum(jnp.where(matches, holder_map[None, :], 0), axis=1)
    slot_hot = slot_of_row[:, None] == jnp.arange(holders, dtype=jnp.int32)[None, :]

    both = jnp.concatenate([adapter_down[0], adapter_up[0]], axis=1)[None]
    both = lax.all_gather(both, DP[-1], axis=0, tiled=False)
    down_w = both[..., :feat_width]
    up_w = both[..., feat_width:]
    for axis in reversed(DP[:-1]):
        down_w = spread_over(down_w, axis)
    down_w = down_w.reshape(holders, rank, feat_width)

    base_bf = base_product(hidden_rows, base_weight)
    base_total = lax.psum_scatter(base_bf, MP, scatter_dimension=1, tiled=True).astype(
        jnp.float32
    )
    up_w, base_total = lax.optimization_barrier((up_w, base_total))
    for axis in reversed(DP[:-1]):
        up_w = lax.all_gather(up_w, axis, axis=0, tiled=False)
    up_w = up_w.reshape(holders, rank, out_width)

    every = jnp.dot(
        hidden_rows,
        down_w.transpose(2, 0, 1).reshape(feat_width, holders * rank),
        preferred_element_type=jnp.float32,
    ).reshape(row_count, holders, rank)
    partial_down = jnp.sum(jnp.where(slot_hot[:, :, None], every, 0.0), axis=1)
    gathered = partial_down.astype(jnp.bfloat16)[None]
    for axis in MP:
        gathered = spread_over(gathered, axis)
    gathered = gathered.reshape(n_mp, row_count, rank)
    down = jnp.sum(gathered.astype(jnp.float32), axis=0).astype(jnp.bfloat16)

    placed = jnp.where(slot_hot[:, :, None], down[:, None, :], jnp.zeros((), jnp.bfloat16))
    lift = jnp.dot(
        placed.reshape(row_count, holders * rank),
        up_w.reshape(holders * rank, out_width),
        preferred_element_type=jnp.float32,
    ).astype(jnp.bfloat16)
    return (base_total + lift.astype(jnp.float32)).astype(jnp.bfloat16)


def coordinate(device, c):
    return device.core_on_chip if c == 3 else device.coords[c]


def fine_mesh(mesh):
    parts = [split_axis(mesh, name) for name in mesh.axis_names]
    names = [tuple(f"{name}{c}" for c, _ in p) for name, p in zip(mesh.axis_names, parts)]
    flat = [q for p in parts for q in p]
    devices = mesh.devices.reshape([n for _, n in flat])
    for k, (c, n) in enumerate(flat):
        for index in np.ndindex(devices.shape):
            if index[k] + 1 < n:
                step = list(index)
                step[k] += 1
                a, b = devices[index], devices[tuple(step)]
                if any((coordinate(a, o) != coordinate(b, o)) != (o == c) for o in range(4)):
                    return mesh, tuple((name,) for name in mesh.axis_names)
    return Mesh(devices, tuple(q for p in names for q in p)), tuple(names)


def solution(mesh):
    global DP, MP
    fine, (DP, MP) = fine_mesh(mesh)
    placed = (
        P(DP, MP),
        P(MP, None),
        P(DP, None, MP),
        P(DP, None, MP),
        P(DP, None),
        P(),
    )
    return jax.shard_map(per_device, mesh=fine, in_specs=placed, out_specs=P(DP, MP), check_vma=False)
```
